512 devices in a mesh: row: 16 (over y, x_lo, core), col: 32 (over z, x_hi).
Axes of the slice: x: 4 (x_hi: 2, x_lo: 2; x = x_hi * 2 + x_lo), y: 4, z: 16, core: 2. Of those that a mesh axis runs over, the one named last changes fastest.
Arguments:
- velocity: bfloat16 [3, 512, 512, 512], P(None, 'row', 'col'), may hold values from -6 to 6
- wall_slope: bfloat16 [512, 512], replicated, may hold values from -0.25 to 0.25
- wall_diffusion: bfloat16 [512, 512], replicated, may hold values from -0.25 to 0.25
- span_slope: bfloat16 [512, 512], replicated, may hold values from -0.25 to 0.25
- span_diffusion: bfloat16 [512, 512], replicated, may hold values from -0.25 to 0.25
Outputs:
- tendency: bfloat16 [3, 512, 512, 512], P(None, 'row', 'col')
The draws below stay inside these ranges and needn't reach their ends.
All inputs are finite; a program needn't handle non-finite values.
Results may differ from the reference program's by a relative error of at most 0.0051.
Values may be sent and summed in bfloat16 or wider, within the bound.
No kernel may reach another device: no remote copies, remote signals or barrier semaphores. Data moves between devices by JAX's collectives and lax.ppermute only.
A program may use at most 128 MiB of HBM per device.

```python
import math
import jax
import jax.numpy as jnp
from jax import lax

NY = 512
NZ = 512
NX = 512


def level_of(own_key, extent, pieces, least, top_value):
    def one(axis_at, blocks):
        steps = jax.random.uniform(jax.random.fold_in(jax.random.fold_in(own_key, 6), axis_at), (blocks,), jnp.float32, least / len(pieces), top_value / len(pieces))
        return jnp.repeat(jnp.exp(steps), extent[axis_at] // blocks).reshape((-1,) + (1,) * (len(extent) - axis_at - 1))

    loudness = one(*pieces[0])
    for cut in pieces[1:]:
        loudness = loudness * one(*cut)
    return loudness


def gaussian(own_key, dims, width, bound, pieces=(), held_as=jnp.bfloat16):
    values = jax.random.normal(own_key, dims, jnp.float32) * width
    if len(pieces) > 0:
        values = level_of(own_key, dims, pieces, -0.22, 0.18) * values
    return jnp.clip(values, min=-bound, max=bound).astype(held_as)


def setup_inputs(seed: int = 0) -> dict:
    key_list = jax.random.split(jax.random.key(seed), 6)
    return {
        "velocity": gaussian(key_list[0], (3, NY, NZ, NX), 1.0, 6.0, ((1, 16), (2, 32))),
        "wall_slope": gaussian(key_list[1], (NY, NY), NY ** -0.5, 0.25),
        "wall_diffusion": gaussian(key_list[2], (NY, NY), NY ** -0.5, 0.25),
        "span_slope": gaussian(key_list[3], (NZ, NZ), NZ ** -0.5, 0.25),
        "span_diffusion": gaussian(key_list[4], (NZ, NZ), NZ ** -0.5, 0.25),
    }


def reference(velocity, wall_slope, wall_diffusion, span_slope, span_diffusion):
    xblock = math.gcd(NX, 32)
    block_count = NX // xblock
    wall_grad = wall_slope.astype(jnp.float32)
    wall_visc = wall_diffusion.astype(jnp.float32)
    span_grad = span_slope.astype(jnp.float32)
    span_visc = span_diffusion.astype(jnp.float32)

    def block_term(offset):
        window_cells = lax.dynamic_slice_in_dim(velocity, offset, xblock, 3).astype(jnp.float32)
        wall_gradient = jnp.einsum('ij,cjzx->cizx', wall_grad, window_cells)
        wall_curvature = jnp.einsum('ij,cjzx->cizx', wall_visc, window_cells)
        wall_term = (wall_curvature - window_cells[1][None] * wall_gradient).astype(jnp.bfloat16)
        span_gradient = jnp.einsum('ij,cyjx->cyix', span_grad, window_cells)
        span_curvature = jnp.einsum('ij,cyjx->cyix', span_visc, window_cells)
        crosswise_contribution = (span_curvature - window_cells[2][None] * span_gradient).astype(jnp.bfloat16)
        wall_term = lax.optimization_barrier(wall_term)
        crosswise_contribution = lax.optimization_barrier(crosswise_contribution)
        return (wall_term.astype(jnp.float32) + crosswise_contribution.astype(jnp.float32)).astype(jnp.bfloat16)

    offsets = jnp.arange(block_count, dtype=jnp.int32) * xblock
    stacked = lax.map(block_term, offsets)
    return jnp.transpose(stacked, (1, 2, 3, 0, 4)).reshape(3, NY, NZ, NX)
```

```python
import jax
import jax.numpy as jnp
from jax import lax
from jax.sharding import PartitionSpec as P


def rate_of_change(slope, diffusion, lines, carrier):
    gradient = jnp.einsum("ij,cjm->cim", slope, lines, preferred_element_type=jnp.float32)
    curvature = jnp.einsum("ij,cjm->cim", diffusion, lines, preferred_element_type=jnp.float32)
    term = curvature - carrier[None].astype(jnp.float32) * gradient
    return term.astype(jnp.bfloat16)


def per_device(velocity, wall_slope, wall_diffusion, span_slope, span_diffusion):
    row_count = lax.axis_size("row")
    column_count = lax.axis_size("col")
    comps, wall_local, span_local, stream_len = velocity.shape
    wall_total = wall_local * row_count
    span_total = span_local * column_count
    span_share = span_local // row_count
    wall_share = wall_local // column_count

    wall_lines = lax.all_to_all(velocity, "row", split_axis=2, concat_axis=1, tiled=True)
    wall_flat = wall_lines.reshape(comps, wall_total, span_share * stream_len)
    wall_term = rate_of_change(wall_slope, wall_diffusion, wall_flat, wall_flat[1])
    wall_back = lax.all_to_all(
        wall_term.reshape(comps, wall_total, span_share, stream_len),
        "row", split_axis=1, concat_axis=2, tiled=True,
    )

    span_lines = lax.all_to_all(velocity, "col", split_axis=1, concat_axis=2, tiled=True)
    span_flat = span_lines.reshape(comps, wall_share, span_total, stream_len)
    span_terms = []
    for w in range(wall_share):
        block = span_flat[:, w]
        span_terms.append(rate_of_change(span_slope, span_diffusion, block, block[2]))
    span_term = jnp.stack(span_terms, axis=1)
    span_back = lax.all_to_all(span_term, "col", split_axis=2, concat_axis=1, tiled=True)

    summed = wall_back.astype(jnp.float32) + span_back.astype(jnp.float32)
    return summed.astype(jnp.bfloat16)


def solution(mesh):
    in_specs = (P(None, "row", "col", None), P(), P(), P(), P())
    out_specs = P(None, "row", "col", None)
    return jax.shard_map(
        per_device, mesh=mesh, in_specs=in_specs, out_specs=out_specs, check_vma=False
    )
```

```python
import jax
import jax.numpy as jnp
from jax import lax
from jax.sharding import PartitionSpec as P


COL_INNER = 2


def rate_of_change(slope, diffusion, lines, carrier):
    gradient = jnp.einsum("ij,cjm->cim", slope, lines, preferred_element_type=jnp.float32)
    curvature = jnp.einsum("ij,cjm->cim", diffusion, lines, preferred_element_type=jnp.float32)
    term = curvature - carrier[None].astype(jnp.float32) * gradient
    return term.astype(jnp.bfloat16)


def col_moves(column_count):
    outer = column_count // COL_INNER
    moves = []
    for dz in range(outer):
        for dx in range(COL_INNER):
            if dz == 0 and dx == 0:
                continue
            pairs = []
            for src in range(column_count):
                z, x = divmod(src, COL_INNER)
                dst = ((z + dz) % outer) * COL_INNER + (x ^ dx)
                pairs.append((src, dst))
            moves.append((dz, dx, pairs))
    return moves


def per_device(velocity, wall_slope, wall_diffusion, span_slope, span_diffusion):
    row_count = lax.axis_size("row")
    column_count = lax.axis_size("col")
    comps, wall_local, span_local, stream_len = velocity.shape
    wall_total = wall_local * row_count
    span_total = span_local * column_count
    span_share = span_local // row_count
    wall_share = wall_local // column_count
    outer = column_count // COL_INNER

    wall_lines = lax.all_to_all(velocity, "row", split_axis=2, concat_axis=1, tiled=True)
    wall_flat = wall_lines.reshape(comps, wall_total, span_share * stream_len)
    wall_term = rate_of_change(wall_slope, wall_diffusion, wall_flat, wall_flat[1])
    wall_back = lax.all_to_all(
        wall_term.reshape(comps, wall_total, span_share, stream_len),
        "row", split_axis=1, concat_axis=2, tiled=True,
    )

    me = lax.axis_index("col")
    mz, mx = me // COL_INNER, me % COL_INNER
    moves = col_moves(column_count)
    by_source = [None] * 1
    pieces = {}
    pieces[0] = lax.dynamic_slice_in_dim(velocity, me * wall_share, wall_share, 1)
    sources = [me]
    for dz, dx, pairs in moves:
        dst = ((mz + dz) % outer) * COL_INNER + (mx ^ dx)
        src = ((mz - dz) % outer) * COL_INNER + (mx ^ dx)
        chunk = lax.dynamic_slice_in_dim(velocity, dst * wall_share, wall_share, 1)
        pieces[len(sources)] = lax.ppermute(chunk, "col", pairs)
        sources.append(src)
    stacked = jnp.stack([pieces[i] for i in range(len(sources))], axis=0)
    source_ids = jnp.stack(sources)
    slot_of_source = jnp.zeros((column_count,), jnp.int32).at[source_ids].set(
        jnp.arange(column_count, dtype=jnp.int32)
    )
    ordered = jnp.take(stacked, slot_of_source, axis=0)
    span_lines = ordered.transpose(1, 2, 0, 3, 4).reshape(comps, wall_share, span_total, stream_len)
    span_terms = []
    for w in range(wall_share):
        block = span_lines[:, w]
        span_terms.append(rate_of_change(span_slope, span_diffusion, block, block[2]))
    span_term = jnp.stack(span_terms, axis=1)

    back = {}
    back[0] = lax.dynamic_slice_in_dim(span_term, me * span_local, span_local, 2)
    for i, (dz, dx, pairs) in enumerate(moves):
        dst = ((mz + dz) % outer) * COL_INNER + (mx ^ dx)
        chunk = lax.dynamic_slice_in_dim(span_term, dst * span_local, span_local, 2)
        back[i + 1] = lax.ppermute(chunk, "col", pairs)
    back_stacked = jnp.stack([back[i] for i in range(len(sources))], axis=0)
    back_ordered = jnp.take(back_stacked, slot_of_source, axis=0)
    span_back = back_ordered.transpose(1, 0, 2, 3, 4).reshape(comps, wall_local, span_local, stream_len)

    summed = wall_back.astype(jnp.float32) + span_back.astype(jnp.float32)
    return summed.astype(jnp.bfloat16)


def solution(mesh):
    in_specs = (P(None, "row", "col", None), P(), P(), P(), P())
    out_specs = P(None, "row", "col", None)
    return jax.shard_map(
        per_device, mesh=mesh, in_specs=in_specs, out_specs=out_specs, check_vma=False
    )
```

```python
import jax
import jax.numpy as jnp
from jax import lax
from jax.sharding import PartitionSpec as P


def per_device(velocity, wall_slope, wall_diffusion, span_slope, span_diffusion):
    row_count = lax.axis_size("row")
    column_count = lax.axis_size("col")
    comps, wall_local, span_local, stream_len = velocity.shape
    wall_total = wall_local * row_count
    span_total = span_local * column_count
    devices = row_count * column_count
    stream_share = stream_len // devices

    outgoing = velocity.reshape(comps, wall_local, span_local, devices, stream_share)
    outgoing = outgoing.transpose(3, 0, 1, 2, 4)
    planes = lax.all_to_all(outgoing, ("row", "col"), split_axis=0, concat_axis=0, tiled=True)
    planes = planes.reshape(row_count, column_count, comps, wall_local, span_local, stream_share)
    planes = planes.transpose(2, 5, 0, 3, 1, 4).reshape(comps, stream_share, wall_total, span_total)

    f32 = jnp.float32
    wall_gradient = jnp.einsum("ij,cxjz->cxiz", wall_slope, planes, preferred_element_type=f32)
    wall_curvature = jnp.einsum("ij,cxjz->cxiz", wall_diffusion, planes, preferred_element_type=f32)
    wall_term = (wall_curvature - planes[1][None].astype(f32) * wall_gradient).astype(jnp.bfloat16)
    span_gradient = jnp.einsum("ij,cxyj->cxyi", span_slope, planes, preferred_element_type=f32)
    span_curvature = jnp.einsum("ij,cxyj->cxyi", span_diffusion, planes, preferred_element_type=f32)
    span_term = (span_curvature - planes[2][None].astype(f32) * span_gradient).astype(jnp.bfloat16)
    summed = (wall_term.astype(f32) + span_term.astype(f32)).astype(jnp.bfloat16)

    homeward = summed.reshape(comps, stream_share, row_count, wall_local, column_count, span_local)
    homeward = homeward.transpose(2, 4, 0, 3, 5, 1).reshape(devices, comps, wall_local, span_local, stream_share)
    back = lax.all_to_all(homeward, ("row", "col"), split_axis=0, concat_axis=0, tiled=True)
    return back.transpose(1, 2, 3, 0, 4).reshape(comps, wall_local, span_local, stream_len)


def solution(mesh):
    in_specs = (P(None, "row", "col", None), P(), P(), P(), P())
    out_specs = P(None, "row", "col", None)
    return jax.shard_map(
        per_device, mesh=mesh, in_specs=in_specs, out_specs=out_specs, check_vma=False
    )
```

```python
import jax
import jax.numpy as jnp
from jax import lax
from jax.sharding import PartitionSpec as P


def rate_of_change(slope, diffusion, lines, carrier):
    gradient = jnp.einsum("ij,cjm->cim", slope, lines, preferred_element_type=jnp.float32)
    curvature = jnp.einsum("ij,cjm->cim", diffusion, lines, preferred_element_type=jnp.float32)
    term = curvature - carrier[None].astype(jnp.float32) * gradient
    return term.astype(jnp.bfloat16)


def exchange(blocks, axis):
    return lax.all_to_all(blocks, axis, split_axis=0, concat_axis=0, tiled=True)


def per_device(velocity, wall_slope, wall_diffusion, span_slope, span_diffusion):
    row_count = lax.axis_size("row")
    column_count = lax.axis_size("col")
    comps, wall_local, span_local, stream_len = velocity.shape
    wall_total = wall_local * row_count
    span_total = span_local * column_count
    zr = span_local // row_count
    ws = wall_local // column_count

    send = velocity.reshape(comps, wall_local, row_count, zr, stream_len).transpose(2, 0, 3, 1, 4)
    got = exchange(send, "row")
    wall_lines = got.transpose(1, 2, 0, 3, 4).reshape(comps, zr, wall_total, stream_len)
    wall_parts = []
    for k in range(zr):
        lines = wall_lines[:, k]
        wall_parts.append(rate_of_change(wall_slope, wall_diffusion, lines, lines[1]))
    wall_term = jnp.stack(wall_parts, axis=1)
    send = wall_term.reshape(comps, zr, row_count, wall_local, stream_len).transpose(2, 0, 1, 3, 4)
    wall_back = exchange(send, "row")
    wall_back = wall_back.transpose(1, 3, 0, 2, 4).reshape(comps, wall_local, span_local, stream_len)

    send = velocity.reshape(comps, column_count, ws, span_local, stream_len).transpose(1, 0, 2, 3, 4)
    got = exchange(send, "col")
    span_lines = got.transpose(1, 2, 0, 3, 4).reshape(comps, ws, span_total, stream_len)
    span_parts = []
    for k in range(ws):
        lines = span_lines[:, k]
        span_parts.append(rate_of_change(span_slope, span_diffusion, lines, lines[2]))
    span_term = jnp.stack(span_parts, axis=1)
    send = span_term.reshape(comps, ws, column_count, span_local, stream_len).transpose(2, 0, 1, 3, 4)
    span_back = exchange(send, "col")
    span_back = span_back.transpose(1, 0, 2, 3, 4).reshape(comps, wall_local, span_local, stream_len)

    summed = wall_back.astype(jnp.float32) + span_back.astype(jnp.float32)
    return summed.astype(jnp.bfloat16)


def solution(mesh):
    in_specs = (P(None, "row", "col", None), P(), P(), P(), P())
    out_specs = P(None, "row", "col", None)
    return jax.shard_map(
        per_device, mesh=mesh, in_specs=in_specs, out_specs=out_specs, check_vma=False
    )
```

```python
import jax
import jax.numpy as jnp
from jax import lax
from jax.sharding import Mesh, PartitionSpec as P

ROW_PARTS = (("y", 4), ("xl", 2), ("core", 2))
COL_PARTS = (("z", 16), ("xh", 2))
NEAR = ("xl", "core")
FAR = ("y", "z", "xh")


def to_bf16_value(x):
    return lax.reduce_precision(x, exponent_bits=8, mantissa_bits=7)


def exchange(blocks, axes):
    return lax.all_to_all(blocks, axes, split_axis=0, concat_axis=0, tiled=True)


def per_device(velocity, wall_slope, wall_diffusion, span_slope, span_diffusion):
    near = lax.axis_size(NEAR)
    ny = lax.axis_size("y")
    nz = lax.axis_size("z")
    nxh = lax.axis_size("xh")
    far = ny * nz * nxh
    comps, wall_local, span_local, stream_len = velocity.shape
    xa = stream_len // near
    xb = xa // far
    wall_group = wall_local * near
    wall_total = wall_group * ny
    span_total = span_local * nz * nxh
    f32 = jnp.float32

    send = velocity.reshape(comps, wall_local, span_local, near, xa).transpose(3, 0, 1, 2, 4)
    got = exchange(send, NEAR)
    send = got.reshape(near, comps, wall_local, span_local, far, xb).transpose(4, 1, 3, 5, 0, 2)
    send = send.reshape(far, comps, span_local, xb, wall_group)
    got = exchange(send, FAR)
    planes = got.reshape(ny, nz, nxh, comps, span_local, xb, wall_group).transpose(3, 5, 1, 2, 4, 0, 6)
    planes = planes.reshape(comps, xb, span_total, wall_total)

    wall_gradient = jnp.einsum("cxzk,yk->cxzy", planes, wall_slope, preferred_element_type=f32)
    wall_curvature = jnp.einsum("cxzk,yk->cxzy", planes, wall_diffusion, preferred_element_type=f32)
    wall_term = to_bf16_value(wall_curvature - planes[1][None].astype(f32) * wall_gradient)
    span_gradient = jnp.einsum("ij,cxjy->cxiy", span_slope, planes, preferred_element_type=f32)
    span_curvature = jnp.einsum("ij,cxjy->cxiy", span_diffusion, planes, preferred_element_type=f32)
    span_term = to_bf16_value(span_curvature - planes[2][None].astype(f32) * span_gradient)
    summed = (wall_term + span_term).astype(jnp.bfloat16)

    send = summed.reshape(comps, xb, nz, nxh, span_local, ny, wall_group).transpose(5, 2, 3, 0, 4, 1, 6)
    send = send.reshape(far, comps, span_local, xb, wall_group)
    got = exchange(send, FAR)
    send = got.reshape(far, comps, span_local, xb, near, wall_local).transpose(4, 1, 5, 2, 0, 3)
    send = send.reshape(near, comps, wall_local, span_local, xa)
    got = exchange(send, NEAR)
    return got.transpose(1, 2, 3, 0, 4).reshape(comps, wall_local, span_local, stream_len)


def solution(mesh):
    names = tuple(n for n, _ in ROW_PARTS + COL_PARTS)
    sizes = tuple(s for _, s in ROW_PARTS + COL_PARTS)
    fine = Mesh(mesh.devices.reshape(sizes), names)
    rows = tuple(n for n, _ in ROW_PARTS)
    cols = tuple(n for n, _ in COL_PARTS)
    in_specs = (P(None, rows, cols, None), P(), P(), P(), P())
    out_specs = P(None, rows, cols, None)
    return jax.shard_map(
        per_device, mesh=fine, in_specs=in_specs, out_specs=out_specs, check_vma=False
    )
```

```python
import jax
import jax.numpy as jnp
from jax import lax
from jax.sharding import Mesh, PartitionSpec as P


ROW_PARTS = (("y", 4), ("xl", 2), ("core", 2))
COL_PARTS = (("z", 16), ("xh", 2))
COLS = ("z", "xh")


def rate_of_change(slope, diffusion, lines, carrier):
    gradient = jnp.einsum("ij,cjm->cim", slope, lines, preferred_element_type=jnp.float32)
    curvature = jnp.einsum("ij,cjm->cim", diffusion, lines, preferred_element_type=jnp.float32)
    term = curvature - carrier[None].astype(jnp.float32) * gradient
    return term.astype(jnp.bfloat16)


def exchange(blocks, axes):
    return lax.all_to_all(blocks, axes, split_axis=0, concat_axis=0, tiled=True)


def take_at(x, i, axis):
    return lax.dynamic_index_in_dim(x, i, axis, keepdims=False)


def swap(x, axis):
    return lax.ppermute(x, axis, [(0, 1), (1, 0)])


def in_order(mine, other, me):
    first = jnp.where(me == 0, mine, other)
    second = jnp.where(me == 0, other, mine)
    return jnp.stack([first, second], axis=0)


def rotate_in(pieces, me, n):
    order = (me - jnp.arange(n)) % n
    return jnp.take(pieces, order, axis=0)


def per_device(velocity, wall_slope, wall_diffusion, span_slope, span_diffusion):
    ny, nxl, ncore = (lax.axis_size(n) for n, _ in ROW_PARTS)
    my_y, my_xl, my_core = (lax.axis_index(n) for n, _ in ROW_PARTS)
    column_count = lax.axis_size(COLS)
    comps, wall_local, span_local, stream_len = velocity.shape
    row_count = ny * nxl * ncore
    wall_total = wall_local * row_count
    span_total = span_local * column_count
    ws = wall_local // column_count
    zr = span_local // row_count

    v = velocity.reshape(comps, wall_local, ny, nxl, ncore, zr, stream_len)
    keep = take_at(v, my_core, 4)
    got = swap(take_at(v, 1 - my_core, 4), "core")
    s1 = in_order(keep, got, my_core)
    keep = take_at(s1, my_xl, 4)
    got = swap(take_at(s1, 1 - my_xl, 4), "xl")
    s2 = in_order(keep, got, my_xl)
    pieces = [take_at(s2, my_y, 4)]
    for s in range(1, ny):
        part = take_at(s2, (my_y + s) % ny, 4)
        pieces.append(lax.ppermute(part, "y", [(i, (i + s) % ny) for i in range(ny)]))
    s3 = rotate_in(jnp.stack(pieces, axis=0), my_y, ny)
    wall_lines = s3.transpose(3, 5, 0, 1, 2, 4, 6).reshape(comps, zr, wall_total, stream_len)
    wall_parts = []
    for k in range(zr):
        lines = wall_lines[:, k]
        wall_parts.append(rate_of_change(wall_slope, wall_diffusion, lines, lines[1]))
    wall_term = jnp.stack(wall_parts, axis=1)

    w = wall_term.reshape(comps, zr, ny, nxl, ncore, wall_local, stream_len)
    pieces = [take_at(w, my_y, 2)]
    for s in range(1, ny):
        part = take_at(w, (my_y + s) % ny, 2)
        pieces.append(lax.ppermute(part, "y", [(i, (i + s) % ny) for i in range(ny)]))
    b3 = rotate_in(jnp.stack(pieces, axis=0), my_y, ny)
    keep = take_at(b3, my_xl, 3)
    got = swap(take_at(b3, 1 - my_xl, 3), "xl")
    b2 = in_order(keep, got, my_xl)
    keep = take_at(b2, my_core, 4)
    got = swap(take_at(b2, 1 - my_core, 4), "core")
    b1 = in_order(keep, got, my_core)
    wall_back = b1.transpose(3, 5, 2, 1, 0, 4, 6).reshape(comps, wall_local, span_local, stream_len)

    send = velocity.reshape(comps, column_count, ws, span_local, stream_len).transpose(1, 0, 2, 3, 4)
    got = exchange(send, COLS)
    span_lines = got.transpose(1, 2, 0, 3, 4).reshape(comps, ws, span_total, stream_len)
    span_parts = []
    for k in range(ws):
        lines = span_lines[:, k]
        span_parts.append(rate_of_change(span_slope, span_diffusion, lines, lines[2]))
    span_term = jnp.stack(span_parts, axis=1)
    send = span_term.reshape(comps, ws, column_count, span_local, stream_len).transpose(2, 0, 1, 3, 4)
    span_back = exchange(send, COLS)
    span_back = span_back.transpose(1, 0, 2, 3, 4).reshape(comps, wall_local, span_local, stream_len)

    summed = wall_back.astype(jnp.float32) + span_back.astype(jnp.float32)
    return summed.astype(jnp.bfloat16)


def solution(mesh):
    names = tuple(n for n, _ in ROW_PARTS + COL_PARTS)
    sizes = tuple(s for _, s in ROW_PARTS + COL_PARTS)
    fine = Mesh(mesh.devices.reshape(sizes), names)
    rows = tuple(n for n, _ in ROW_PARTS)
    in_specs = (P(None, rows, COLS, None), P(), P(), P(), P())
    out_specs = P(None, rows, COLS, None)
    return jax.shard_map(
        per_device, mesh=fine, in_specs=in_specs, out_specs=out_specs, check_vma=False
    )
```

```python
import jax
import jax.numpy as jnp
from jax import lax
from jax.experimental import pallas as pl
from jax.sharding import Mesh, PartitionSpec as P


ROW_PARTS = (("y", 4), ("xl", 2), ("core", 2))
COL_PARTS = (("z", 16), ("xh", 2))
COLS = ("z", "xh")


def rate_of_change(slope, diffusion, lines, carrier):
    gradient = jnp.einsum("ij,cjm->cim", slope, lines, preferred_element_type=jnp.float32)
    curvature = jnp.einsum("ij,cjm->cim", diffusion, lines, preferred_element_type=jnp.float32)
    term = curvature - carrier[None].astype(jnp.float32) * gradient
    return term.astype(jnp.bfloat16)


def span_kernel(lines_ref, carrier_ref, slope_ref, diffusion_ref, out_ref):
    src, _, cells, stream = lines_ref.shape
    lines = lines_ref[:, 0].reshape(src * cells, stream)
    carrier = carrier_ref[:, 0].reshape(src * cells, stream).astype(jnp.float32)
    gradient = jnp.dot(slope_ref[...], lines, preferred_element_type=jnp.float32)
    curvature = jnp.dot(diffusion_ref[...], lines, preferred_element_type=jnp.float32)
    term = (curvature - carrier * gradient).astype(jnp.bfloat16)
    out_ref[:, 0] = term.reshape(src, cells, stream)


def span_terms(got, span_slope, span_diffusion, carrier_comp):
    src, planes, cells, stream = got.shape
    ws = planes // 3
    block = pl.BlockSpec((src, 1, cells, stream), lambda j: (0, j, 0, 0))
    carrier = pl.BlockSpec((src, 1, cells, stream), lambda j: (0, carrier_comp * ws + j % ws, 0, 0))
    full = pl.BlockSpec(span_slope.shape, lambda j: (0, 0))
    return pl.pallas_call(
        span_kernel,
        grid=(planes,),
        in_specs=[block, carrier, full, full],
        out_specs=block,
        out_shape=jax.ShapeDtypeStruct(got.shape, got.dtype),
    )(got, got, span_slope, span_diffusion)


def add_kernel(wall_ref, span_ref, out_ref):
    src, _, ws, cells, stream = span_ref.shape
    span = span_ref[:, 0].reshape(src * ws, cells, stream).astype(jnp.float32)
    wall = wall_ref[0].astype(jnp.float32)
    out_ref[0] = (wall + span).astype(jnp.bfloat16)


def add_terms(wall_back, span_back):
    comps, wall_local, span_local, stream = wall_back.shape
    src, _, ws, _, _ = span_back.shape
    out_block = pl.BlockSpec((1, wall_local, span_local, stream), lambda c: (c, 0, 0, 0))
    span_block = pl.BlockSpec((src, 1, ws, span_local, stream), lambda c: (0, c, 0, 0, 0))
    return pl.pallas_call(
        add_kernel,
        grid=(comps,),
        in_specs=[out_block, span_block],
        out_specs=out_block,
        out_shape=jax.ShapeDtypeStruct(wall_back.shape, wall_back.dtype),
    )(wall_back, span_back)


def exchange(blocks, axes):
    return lax.all_to_all(blocks, axes, split_axis=0, concat_axis=0, tiled=True)


def take_at(x, i, axis):
    return lax.dynamic_index_in_dim(x, i, axis, keepdims=False)


def swap(x, axis):
    return lax.ppermute(x, axis, [(0, 1), (1, 0)])


def in_order(mine, other, me):
    first = jnp.where(me == 0, mine, other)
    second = jnp.where(me == 0, other, mine)
    return jnp.stack([first, second], axis=0)


def rotate_in(pieces, me, n):
    order = (me - jnp.arange(n)) % n
    return jnp.take(pieces, order, axis=0)


def both_terms(velocity, wall_slope, wall_diffusion, span_slope, span_diffusion):
    ny, nxl, ncore = (lax.axis_size(n) for n, _ in ROW_PARTS)
    my_y, my_xl, my_core = (lax.axis_index(n) for n, _ in ROW_PARTS)
    column_count = lax.axis_size(COLS)
    comps, wall_local, span_local, stream_len = velocity.shape
    row_count = ny * nxl * ncore
    wall_total = wall_local * row_count
    ws = wall_local // column_count
    zr = span_local // row_count

    v = velocity.reshape(comps, wall_local, ny, nxl, ncore, zr, stream_len)
    keep = take_at(v, my_core, 4)
    got = swap(take_at(v, 1 - my_core, 4), "core")
    s1 = in_order(keep, got, my_core)
    keep = take_at(s1, my_xl, 4)
    got = swap(take_at(s1, 1 - my_xl, 4), "xl")
    s2 = in_order(keep, got, my_xl)
    pieces = [take_at(s2, my_y, 4)]
    for s in range(1, ny):
        part = take_at(s2, (my_y + s) % ny, 4)
        pieces.append(lax.ppermute(part, "y", [(i, (i + s) % ny) for i in range(ny)]))
    s3 = rotate_in(jnp.stack(pieces, axis=0), my_y, ny)
    wall_lines = s3.transpose(3, 5, 0, 1, 2, 4, 6).reshape(comps, zr, wall_total, stream_len)

    wall_parts = []
    for k in range(zr):
        lines = wall_lines[:, k]
        wall_parts.append(rate_of_change(wall_slope, wall_diffusion, lines, lines[1]))
    wall_term = jnp.stack(wall_parts, axis=1)

    w = wall_term.reshape(comps, zr, ny, nxl, ncore, wall_local, stream_len)
    pieces = [take_at(w, my_y, 2)]
    for s in range(1, ny):
        part = take_at(w, (my_y + s) % ny, 2)
        pieces.append(lax.ppermute(part, "y", [(i, (i + s) % ny) for i in range(ny)]))
    b3 = rotate_in(jnp.stack(pieces, axis=0), my_y, ny)
    keep = take_at(b3, my_xl, 3)
    got = swap(take_at(b3, 1 - my_xl, 3), "xl")
    b2 = in_order(keep, got, my_xl)
    keep = take_at(b2, my_core, 4)
    got = swap(take_at(b2, 1 - my_core, 4), "core")
    b1 = in_order(keep, got, my_core)
    wall_back = b1.transpose(3, 5, 2, 1, 0, 4, 6).reshape(comps, wall_local, span_local, stream_len)

    send = velocity.reshape(comps, column_count, ws, span_local, stream_len).transpose(1, 0, 2, 3, 4)
    got = exchange(send, COLS)
    got = got.reshape(column_count, comps * ws, span_local, stream_len)
    send = span_terms(got, span_slope, span_diffusion, 2)
    send = send.reshape(column_count, comps, ws, span_local, stream_len)
    span_back = exchange(send, COLS)
    return add_terms(wall_back, span_back)


def solution(mesh):
    names = tuple(n for n, _ in ROW_PARTS + COL_PARTS)
    sizes = tuple(s for _, s in ROW_PARTS + COL_PARTS)
    fine = Mesh(mesh.devices.reshape(sizes), names)
    rows = tuple(n for n, _ in ROW_PARTS)
    in_specs = (P(None, rows, COLS, None), P(), P(), P(), P())
    out_specs = P(None, rows, COLS, None)
    return jax.shard_map(
        both_terms, mesh=fine, in_specs=in_specs, out_specs=out_specs, check_vma=False
    )
```

```python
import jax
import jax.numpy as jnp
from jax import lax
from jax.sharding import Mesh, PartitionSpec as P


ROW_PARTS = (("y", 4), ("xl", 2), ("core", 2))
COL_PARTS = (("z", 16), ("xh", 2))
COLS = ("z", "xh")


def rate_of_change(slope, diffusion, lines, carrier):
    gradient = jnp.einsum("ij,cjm->cim", slope, lines, preferred_element_type=jnp.float32)
    curvature = jnp.einsum("ij,cjm->cim", diffusion, lines, preferred_element_type=jnp.float32)
    term = curvature - carrier[None].astype(jnp.float32) * gradient
    return term.astype(jnp.bfloat16)


def exchange(blocks, axes):
    return lax.all_to_all(blocks, axes, split_axis=0, concat_axis=0, tiled=True)


def take_at(x, i, axis):
    return lax.dynamic_index_in_dim(x, i, axis, keepdims=False)


def swap(x, axis):
    return lax.ppermute(x, axis, [(0, 1), (1, 0)])


def in_order(mine, other, me):
    first = jnp.where(me == 0, mine, other)
    second = jnp.where(me == 0, other, mine)
    return jnp.stack([first, second], axis=0)


def rotate_in(pieces, me, n):
    order = (me - jnp.arange(n)) % n
    return jnp.take(pieces, order, axis=0)


def both_terms(velocity, wall_slope, wall_diffusion, span_slope, span_diffusion):
    ny, nxl, ncore = (lax.axis_size(n) for n, _ in ROW_PARTS)
    my_y, my_xl, my_core = (lax.axis_index(n) for n, _ in ROW_PARTS)
    column_count = lax.axis_size(COLS)
    comps, wall_local, span_local, stream_len = velocity.shape
    row_count = ny * nxl * ncore
    wall_total = wall_local * row_count
    span_total = span_local * column_count
    ws = wall_local // column_count
    zr = span_local // row_count

    v = velocity.reshape(comps, wall_local, ny, nxl, ncore, zr, stream_len)
    keep = take_at(v, my_core, 4)
    got = swap(take_at(v, 1 - my_core, 4), "core")
    s1 = in_order(keep, got, my_core)
    keep = take_at(s1, my_xl, 4)
    got = swap(take_at(s1, 1 - my_xl, 4), "xl")
    s2 = in_order(keep, got, my_xl)
    pieces = [take_at(s2, my_y, 4)]
    for s in range(1, ny):
        part = take_at(s2, (my_y + s) % ny, 4)
        pieces.append(lax.ppermute(part, "y", [(i, (i + s) % ny) for i in range(ny)]))
    s3 = rotate_in(jnp.stack(pieces, axis=0), my_y, ny)
    wall_lines = s3.transpose(3, 5, 0, 1, 2, 4, 6).reshape(comps, zr, wall_total, stream_len)

    wall_parts = []
    for k in range(zr):
        lines = wall_lines[:, k]
        wall_parts.append(rate_of_change(wall_slope, wall_diffusion, lines, lines[1]))
    wall_term = jnp.stack(wall_parts, axis=1)

    w = wall_term.reshape(comps, zr, ny, nxl, ncore, wall_local, stream_len)
    pieces = [take_at(w, my_y, 2)]
    for s in range(1, ny):
        part = take_at(w, (my_y + s) % ny, 2)
        pieces.append(lax.ppermute(part, "y", [(i, (i + s) % ny) for i in range(ny)]))
    b3 = rotate_in(jnp.stack(pieces, axis=0), my_y, ny)
    keep = take_at(b3, my_xl, 3)
    got = swap(take_at(b3, 1 - my_xl, 3), "xl")
    b2 = in_order(keep, got, my_xl)
    keep = take_at(b2, my_core, 4)
    got = swap(take_at(b2, 1 - my_core, 4), "core")
    b1 = in_order(keep, got, my_core)
    wall_back = b1.transpose(3, 5, 2, 1, 0, 4, 6).reshape(comps, wall_local, span_local, stream_len)

    send = velocity.reshape(comps, column_count, ws, span_local, stream_len).transpose(1, 0, 2, 3, 4)
    got = exchange(send, COLS)
    span_lines = got.transpose(1, 2, 0, 3, 4).reshape(comps, ws, span_total, stream_len)
    span_parts = []
    for k in range(ws):
        lines = span_lines[:, k]
        span_parts.append(rate_of_change(span_slope, span_diffusion, lines, lines[2]))
    span_term = jnp.stack(span_parts, axis=1)
    send = span_term.reshape(comps, ws, column_count, span_local, stream_len).transpose(2, 0, 1, 3, 4)
    span_back = exchange(send, COLS)
    span_back = span_back.transpose(1, 0, 2, 3, 4).reshape(comps, wall_local, span_local, stream_len)

    summed = wall_back.astype(jnp.float32) + span_back.astype(jnp.float32)
    return summed.astype(jnp.bfloat16)


def solution(mesh):
    names = tuple(n for n, _ in ROW_PARTS + COL_PARTS)
    sizes = tuple(s for _, s in ROW_PARTS + COL_PARTS)
    fine = Mesh(mesh.devices.reshape(sizes), names)
    rows = tuple(n for n, _ in ROW_PARTS)
    in_specs = (P(None, rows, COLS, None), P(), P(), P(), P())
    out_specs = P(None, rows, COLS, None)
    return jax.shard_map(both_terms, mesh=fine, in_specs=in_specs, out_specs=out_specs, check_vma=False)
```

```python
import jax
import jax.numpy as jnp
from jax import lax
from jax.experimental import pallas as pl
from jax.sharding import Mesh, PartitionSpec as P


ROW_PARTS = (("y", 4), ("xl", 2), ("core", 2))
COL_PARTS = (("z", 16), ("xh", 2))
COLS = ("z", "xh")


def rate_of_change(slope, diffusion, lines, carrier):
    gradient = jnp.einsum("ij,cjm->cim", slope, lines, preferred_element_type=jnp.float32)
    curvature = jnp.einsum("ij,cjm->cim", diffusion, lines, preferred_element_type=jnp.float32)
    term = curvature - carrier[None].astype(jnp.float32) * gradient
    return term.astype(jnp.bfloat16)


def copy_kernel(src_ref, out_ref):
    out_ref[...] = src_ref[...]


def in_output_layout(x):
    block = pl.BlockSpec((1,) + x.shape[1:], lambda c: (c,) + (0,) * (x.ndim - 1))
    return pl.pallas_call(
        copy_kernel,
        grid=(x.shape[0],),
        in_specs=[block],
        out_specs=block,
        out_shape=jax.ShapeDtypeStruct(x.shape, x.dtype),
    )(x)


def exchange(blocks, axes):
    return lax.all_to_all(blocks, axes, split_axis=0, concat_axis=0, tiled=True)


def take_at(x, i, axis):
    return lax.dynamic_index_in_dim(x, i, axis, keepdims=False)


def swap(x, axis):
    return lax.ppermute(x, axis, [(0, 1), (1, 0)])


def in_order(mine, other, me):
    first = jnp.where(me == 0, mine, other)
    second = jnp.where(me == 0, other, mine)
    return jnp.stack([first, second], axis=0)


def rotate_in(pieces, me, n):
    order = (me - jnp.arange(n)) % n
    return jnp.take(pieces, order, axis=0)


def both_terms(velocity, wall_slope, wall_diffusion, span_slope, span_diffusion):
    ny, nxl, ncore = (lax.axis_size(n) for n, _ in ROW_PARTS)
    my_y, my_xl, my_core = (lax.axis_index(n) for n, _ in ROW_PARTS)
    column_count = lax.axis_size(COLS)
    comps, wall_local, span_local, stream_len = velocity.shape
    row_count = ny * nxl * ncore
    wall_total = wall_local * row_count
    span_total = span_local * column_count
    ws = wall_local // column_count
    zr = span_local // row_count

    v = velocity.reshape(comps, wall_local, ny, nxl, ncore, zr, stream_len)
    keep = take_at(v, my_core, 4)
    got = swap(take_at(v, 1 - my_core, 4), "core")
    s1 = in_order(keep, got, my_core)
    keep = take_at(s1, my_xl, 4)
    got = swap(take_at(s1, 1 - my_xl, 4), "xl")
    s2 = in_order(keep, got, my_xl)
    pieces = [take_at(s2, my_y, 4)]
    for s in range(1, ny):
        part = take_at(s2, (my_y + s) % ny, 4)
        pieces.append(lax.ppermute(part, "y", [(i, (i + s) % ny) for i in range(ny)]))
    s3 = rotate_in(jnp.stack(pieces, axis=0), my_y, ny)
    wall_lines = s3.transpose(3, 5, 0, 1, 2, 4, 6).reshape(comps, zr, wall_total, stream_len)

    wall_parts = []
    for k in range(zr):
        lines = wall_lines[:, k]
        wall_parts.append(rate_of_change(wall_slope, wall_diffusion, lines, lines[1]))
    wall_term = jnp.stack(wall_parts, axis=1)

    w = wall_term.reshape(comps, zr, ny, nxl, ncore, wall_local, stream_len)
    pieces = [take_at(w, my_y, 2)]
    for s in range(1, ny):
        part = take_at(w, (my_y + s) % ny, 2)
        pieces.append(lax.ppermute(part, "y", [(i, (i + s) % ny) for i in range(ny)]))
    b3 = rotate_in(jnp.stack(pieces, axis=0), my_y, ny)
    keep = take_at(b3, my_xl, 3)
    got = swap(take_at(b3, 1 - my_xl, 3), "xl")
    b2 = in_order(keep, got, my_xl)
    keep = take_at(b2, my_core, 4)
    got = swap(take_at(b2, 1 - my_core, 4), "core")
    b1 = in_order(keep, got, my_core)
    wall_back = b1.transpose(3, 5, 2, 1, 0, 4, 6).reshape(comps, wall_local, span_local, stream_len)
    wall_back = in_output_layout(wall_back)

    send = velocity.reshape(comps, column_count, ws, span_local, stream_len).transpose(1, 0, 2, 3, 4)
    got = exchange(send, COLS)
    span_lines = got.transpose(1, 2, 0, 3, 4).reshape(comps, ws, span_total, stream_len)
    span_parts = []
    for k in range(ws):
        lines = span_lines[:, k]
        span_parts.append(rate_of_change(span_slope, span_diffusion, lines, lines[2]))
    span_term = jnp.stack(span_parts, axis=1)
    send = span_term.reshape(comps, ws, column_count, span_local, stream_len).transpose(2, 0, 1, 3, 4)
    span_back = exchange(send, COLS)
    span_back = span_back.transpose(1, 0, 2, 3, 4).reshape(comps, wall_local, span_local, stream_len)

    summed = wall_back.astype(jnp.float32) + span_back.astype(jnp.float32)
    return summed.astype(jnp.bfloat16)


def solution(mesh):
    names = tuple(n for n, _ in ROW_PARTS + COL_PARTS)
    sizes = tuple(s for _, s in ROW_PARTS + COL_PARTS)
    fine = Mesh(mesh.devices.reshape(sizes), names)
    rows = tuple(n for n, _ in ROW_PARTS)
    in_specs = (P(None, rows, COLS, None), P(), P(), P(), P())
    out_specs = P(None, rows, COLS, None)
    return jax.shard_map(both_terms, mesh=fine, in_specs=in_specs, out_specs=out_specs, check_vma=False)
```
